128 devices in a mesh: line: 16 (over z, x_lo, core), col: 8 (over x_hi, y).
Axes of the slice: x: 4 (x_hi: 2, x_lo: 2; x = x_hi * 2 + x_lo), y: 4, z: 4, core: 2. Of those that a mesh axis runs over, the one named last changes fastest.
Arguments:
- ptdf: bfloat16 [12288, 36864], P('line', 'col'), may hold values from -0.03125 to 0.03125
- lodf: bfloat16 [12288, 12288], P('line', 'col'), may hold values from -3.296875 to 3.296875
- injection: float32 [512, 36864], P('line', 'col'), may hold values from 0 to 1
- injection_prev: float32 [512, 36864], P('line', 'col'), may hold values from 0 to 1
- bus_cost: float32 [36864], P('col'), may hold values from -1 to 1
- bus_cap: float32 [36864], P('col'), may hold values from 0.5 to 2
- demand: float32 [512], P('line'), may hold values from 12902.4 to 23961.6
- balance_dual: float32 [512], P('line'), may hold values from -3 to 3
- base_dual: float32 [512, 12288], P(None, 'line'), may hold values from -3 to 3
- post_dual: float32 [512, 12288], P(None, 'line'), may hold values from -3 to 3
- flow_limit: float32 [12288], P('line'), may hold values from 0.3 to 2
- emergency_limit: float32 [12288], P('line'), may hold values from 0.4 to 2.5
- outage_line: int32 [12288], P('col'), may hold values from 0 to 12287, each once
- outage_weight: float32 [12288], P('col'), may hold values from 0.004961604 to 0.059539247
Outputs:
- new_injection: float32 [512, 36864], P('line', 'col')
- balance_new: float32 [512], P('line')
- base_new: float32 [512, 12288], P(None, 'line')
- post_new: float32 [512, 12288], P(None, 'line')
The draws below stay inside these ranges and needn't reach their ends.
Inputs may be any that keep to these rules, and one draw needn't show every extreme that they name: `outage_line`: a permutation: every line is the outage of exactly one contingency.
All inputs are finite; a program needn't handle non-finite values.
Results may differ from the reference program's by a relative error of at most 0.0075.
Values may be sent and summed in bfloat16 or wider, within the bound.
No kernel may reach another device: no remote copies, remote signals or barrier semaphores. Data moves between devices by JAX's collectives and lax.ppermute only.
A program may use at most 192 MiB of HBM per device.

```python
import math
import jax
import jax.numpy as jnp

LINES = 12288
BUSES = 36864
SNAPSHOTS = 512


def shard_levels(key, extent, split, low, high):
    gain, own = 1.0, jax.random.fold_in(key, 6)
    for axis_at, shards_of in split:
        heights = jnp.exp(jax.random.uniform(jax.random.fold_in(own, axis_at), (shards_of,), jnp.float32, low / len(split), high / len(split)))
        gain = gain * jnp.repeat(heights, extent[axis_at] // shards_of).reshape([-1 if axis == axis_at else 1 for axis in range(len(extent))])
    return gain


def normal_values(own_key, shape, deviation, most, shards=(), kind=jnp.bfloat16):
    values = jax.random.normal(own_key, shape, jnp.float32) * deviation
    if len(shards) > 0:
        values = shard_levels(own_key, shape, shards, -0.22, 0.18) * values
    return jnp.clip(values, min=-most, max=most).astype(kind)


def setup_inputs(seed: int = 0) -> dict:
    seeds = jax.random.split(jax.random.key(seed), 15)
    return {
        "ptdf": normal_values(seeds[0], (LINES, BUSES), BUSES ** -0.5, 0.03125, ((0, 16), (1, 8))),
        "lodf": normal_values(seeds[1], (LINES, LINES), 0.3, 3.296875, ((0, 16), (1, 8))),
        "injection": jnp.clip(1.0 * jax.random.uniform(seeds[2], (SNAPSHOTS, BUSES), jnp.float32) ** shard_levels(seeds[2], (SNAPSHOTS, BUSES), ((0, 16), (1, 8)), -0.2, 0.2), 0.0, 1.0),
        "injection_prev": jnp.clip(1.0 * jax.random.uniform(seeds[3], (SNAPSHOTS, BUSES), jnp.float32) ** shard_levels(seeds[3], (SNAPSHOTS, BUSES), ((0, 16), (1, 8)), -0.2, 0.2), 0.0, 1.0),
        "bus_cost": jnp.clip(jax.random.uniform(seeds[4], (BUSES,), jnp.float32, -1.0, 1.0) * shard_levels(seeds[4], (BUSES,), ((0, 8),), -0.4, 0.0), -1.0, 1.0),
        "bus_cap": jnp.clip(jnp.exp(math.log(2.0) - 1.3862944 * jax.random.uniform(seeds[5], (BUSES,), jnp.float32) ** shard_levels(seeds[5], (BUSES,), ((0, 8),), -0.2, 0.2)), 0.5, 2.0),
        "demand": jnp.clip(12902.4 + 11059.199 * jax.random.uniform(seeds[6], (SNAPSHOTS,), jnp.float32) ** shard_levels(seeds[6], (SNAPSHOTS,), ((0, 16),), -0.2, 0.2), 12902.4, 23961.6),
        "balance_dual": normal_values(seeds[7], (SNAPSHOTS,), 0.5, 3.0, ((0, 16),), jnp.float32),
        "base_dual": normal_values(seeds[8], (SNAPSHOTS, LINES), 0.5, 3.0, ((1, 16),), jnp.float32),
        "post_dual": normal_values(seeds[9], (SNAPSHOTS, LINES), 0.5, 3.0, ((1, 16),), jnp.float32),
        "flow_limit": jnp.clip(jnp.exp(math.log(2.0) - 1.89712 * jax.random.uniform(seeds[10], (LINES,), jnp.float32) ** shard_levels(seeds[10], (LINES,), ((0, 16),), -0.2, 0.2)), 0.3, 2.0),
        "emergency_limit": jnp.clip(jnp.exp(math.log(2.5) - 1.8325814 * jax.random.uniform(seeds[11], (LINES,), jnp.float32) ** shard_levels(seeds[11], (LINES,), ((0, 16),), -0.2, 0.2)), 0.4, 2.5),
        "outage_line": jax.random.permutation(seeds[12], LINES).astype(jnp.int32),
        "outage_weight": jnp.clip(jnp.exp(math.log(0.059539247) - 2.4849067 * jax.random.uniform(seeds[13], (LINES,), jnp.float32) ** shard_levels(seeds[13], (LINES,), ((0, 8),), -0.2, 0.2)), 0.004961604, 0.059539247),
    }


dual_step = 0.5
primal_step = 0.5


def dual_update(dual, flow, limit):
    shifted = dual + dual_step * flow
    return shifted - dual_step * jnp.clip(shifted / dual_step, -limit, limit)


def reference(ptdf, lodf, injection, injection_prev, bus_cost, bus_cap, demand, balance_dual, base_dual, post_dual, flow_limit, emergency_limit, outage_line, outage_weight):
    extrapolated = 2.0 * injection - injection_prev
    extra_high = extrapolated.astype(jnp.bfloat16)
    extra_low = (extrapolated - extra_high.astype(jnp.float32)).astype(jnp.bfloat16)
    base_flow = jnp.dot(extra_high, ptdf.T, preferred_element_type=jnp.float32) + jnp.dot(extra_low, ptdf.T, preferred_element_type=jnp.float32)
    bus_total = jnp.sum(extra_high.astype(jnp.float32) + extra_low.astype(jnp.float32), axis=1)
    balance_new = balance_dual + (bus_total - demand) / BUSES
    base_new = dual_update(base_dual, base_flow, flow_limit[None, :])
    outage_flow = (jnp.take(base_flow, outage_line, axis=1) * outage_weight[None, :]).astype(jnp.bfloat16)
    post_shift = jnp.dot(outage_flow, lodf.T, preferred_element_type=jnp.float32)
    post_flow = base_flow + post_shift
    post_new = dual_update(post_dual, post_flow, emergency_limit[None, :])
    back_flow = jnp.dot(post_new.astype(jnp.bfloat16), lodf, preferred_element_type=jnp.float32)
    returned = jnp.zeros(base_new.shape, base_new.dtype).at[:, outage_line].add(back_flow * outage_weight[None, :])
    line_total = (base_new + post_new + returned).astype(jnp.bfloat16)
    prices = jnp.dot(line_total, ptdf, preferred_element_type=jnp.float32)
    moved = injection - primal_step * (bus_cost[None, :] + prices + balance_new[:, None])
    new_injection = jnp.clip(moved, 0.0, bus_cap[None, :])
    return new_injection, balance_new, base_new, post_new
```

```python
import jax
import jax.numpy as jnp
from jax import lax
from jax.sharding import PartitionSpec as P

BUSES = 36864


dual_step = 0.5
primal_step = 0.5


def dual_update(dual, flow, limit):
    shifted = dual + dual_step * flow
    return shifted - dual_step * jnp.clip(shifted / dual_step, -limit, limit)


def on_device(
    ptdf,
    lodf,
    injection,
    injection_prev,
    bus_cost,
    bus_cap,
    demand,
    balance_dual,
    base_dual,
    post_dual,
    flow_limit,
    emergency_limit,
    outage_line,
    outage_weight,
):
    extrapolated = 2.0 * injection - injection_prev
    extra_high = extrapolated.astype(jnp.bfloat16)
    extra_low = (extrapolated - extra_high.astype(jnp.float32)).astype(jnp.bfloat16)
    stacked = jnp.stack([extra_high, extra_low], axis=0)
    lines_dev = ptdf.shape[0]
    ptdf_turned = ptdf.T
    portion = lax.all_gather(stacked, "line", axis=1, tiled=True)
    count = portion.shape[1]
    flat = portion.reshape(2 * count, portion.shape[2])
    product = jnp.dot(flat, ptdf_turned, preferred_element_type=jnp.float32)
    flow_part = product[:count] + product[count:]
    local_total = jnp.sum(extra_high.astype(jnp.float32) + extra_low.astype(jnp.float32), axis=1)
    bus_total = lax.psum(local_total, "col")
    base_flow = lax.psum(flow_part, "col")
    balance_new = balance_dual + (bus_total - demand) / BUSES
    base_new = dual_update(base_dual, base_flow, flow_limit[None, :])
    first_line = lax.axis_index("line") * lines_dev
    local_line = outage_line - first_line
    inside = (local_line >= 0) & (local_line < lines_dev)
    safe_line = jnp.where(inside, local_line, 0)
    picked = jnp.take(base_flow, safe_line, axis=1)
    weighted = jnp.where(inside[None, :], picked * outage_weight[None, :], 0.0)
    pieces = lax.psum_scatter(weighted.astype(jnp.bfloat16), "line", scatter_dimension=0, tiled=True)
    outage_flow = lax.all_gather(pieces, "line", axis=0, tiled=True)
    shift_part = jnp.dot(outage_flow, lodf.T, preferred_element_type=jnp.float32)
    post_shift = lax.psum(shift_part, "col")
    post_flow = base_flow + post_shift
    post_new = dual_update(post_dual, post_flow, emergency_limit[None, :])
    back_part = jnp.dot(post_new.astype(jnp.bfloat16), lodf, preferred_element_type=jnp.float32)
    back_flow = lax.psum(back_part, "line")
    target = jnp.where(inside, local_line, lines_dev)
    returned_part = (
        jnp.zeros(base_new.shape, jnp.float32)
        .at[:, target]
        .add(back_flow * outage_weight[None, :], mode="drop")
    )
    returned = lax.psum(returned_part, "col")
    line_total = (base_new + post_new + returned).astype(jnp.bfloat16)
    prices = lax.psum_scatter(
        jnp.dot(line_total, ptdf, preferred_element_type=jnp.float32),
        "line",
        scatter_dimension=0,
        tiled=True,
    )
    moved = injection - primal_step * (bus_cost[None, :] + prices + balance_new[:, None])
    new_injection = jnp.clip(moved, 0.0, bus_cap[None, :])
    return (new_injection, balance_new, base_new, post_new)


def solution(mesh):
    in_specs = (
        P("line", "col"),
        P("line", "col"),
        P("line", "col"),
        P("line", "col"),
        P("col"),
        P("col"),
        P("line"),
        P("line"),
        P(None, "line"),
        P(None, "line"),
        P("line"),
        P("line"),
        P("col"),
        P("col"),
    )
    out_specs = (P("line", "col"), P("line"), P(None, "line"), P(None, "line"))
    return jax.shard_map(
        on_device, mesh=mesh, in_specs=in_specs, out_specs=out_specs, check_vma=False
    )
```

```python
import jax
import jax.numpy as jnp
from jax import lax
from jax.sharding import PartitionSpec as P

BUSES = 36864
CHUNKS = 2


dual_step = 0.5
primal_step = 0.5


def dual_update(dual, flow, limit):
    shifted = dual + dual_step * flow
    return shifted - dual_step * jnp.clip(shifted / dual_step, -limit, limit)


def tie(value, previous):
    if previous is None:
        return value
    value, _ = lax.optimization_barrier((value, previous))
    return value


def pipeline(
    extra_high,
    extra_low,
    injection,
    bus_cost,
    bus_cap,
    balance_new,
    base_dual,
    post_dual,
    flow_limit,
    emergency_limit,
    ptdf,
    lodf,
    inside,
    safe_line,
    target,
    outage_weight,
):
    chunks = range(len(extra_high))
    base_flow, outage_flow, post_new, base_new, back_flow, returned = [], [], [], [], [], []
    last_col = None
    for c in chunks:
        stacked = jnp.stack([extra_high[c], extra_low[c]], axis=0)
        portion = lax.all_gather(stacked, "line", axis=1, tiled=True)
        count = portion.shape[1]
        flat = portion.reshape(2 * count, portion.shape[2])
        product = jnp.dot(flat, ptdf.T, preferred_element_type=jnp.float32)
        flow_part = product[:count] + product[count:]
        last_col = lax.psum(tie(flow_part, last_col), "col")
        base_flow.append(last_col)
    for c in chunks:
        base_new.append(dual_update(base_dual[c], base_flow[c], flow_limit[None, :]))
        picked = jnp.take(base_flow[c], safe_line, axis=1)
        weighted = jnp.where(inside[None, :], picked * outage_weight[None, :], 0.0)
        pieces = lax.psum_scatter(weighted.astype(jnp.bfloat16), "line", scatter_dimension=0, tiled=True)
        outage_flow.append(lax.all_gather(pieces, "line", axis=0, tiled=True))
    for c in chunks:
        shift_part = jnp.dot(outage_flow[c], lodf.T, preferred_element_type=jnp.float32)
        post_shift = lax.psum(tie(shift_part, last_col), "col")
        last_col = post_shift
        post_flow = base_flow[c] + post_shift
        post_new.append(dual_update(post_dual[c], post_flow, emergency_limit[None, :]))
    for c in chunks:
        back_part = jnp.dot(post_new[c].astype(jnp.bfloat16), lodf, preferred_element_type=jnp.float32)
        back_flow.append(lax.psum(tie(back_part, back_flow[c - 1] if c else None), "line"))
    for c in chunks:
        returned_part = (
            jnp.zeros(base_new[c].shape, jnp.float32)
            .at[:, target]
            .add(back_flow[c] * outage_weight[None, :], mode="drop")
        )
        last_col = lax.psum(tie(returned_part, last_col), "col")
        returned.append(last_col)
    new_injection = []
    for c in chunks:
        line_total = (base_new[c] + post_new[c] + returned[c]).astype(jnp.bfloat16)
        prices = lax.psum_scatter(
            jnp.dot(line_total, ptdf, preferred_element_type=jnp.float32),
            "line",
            scatter_dimension=0,
            tiled=True,
        )
        moved = injection[c] - primal_step * (bus_cost[None, :] + prices + balance_new[c][:, None])
        new_injection.append(jnp.clip(moved, 0.0, bus_cap[None, :]))
    return new_injection, base_new, post_new


def on_device(
    ptdf,
    lodf,
    injection,
    injection_prev,
    bus_cost,
    bus_cap,
    demand,
    balance_dual,
    base_dual,
    post_dual,
    flow_limit,
    emergency_limit,
    outage_line,
    outage_weight,
):
    extrapolated = 2.0 * injection - injection_prev
    extra_high = extrapolated.astype(jnp.bfloat16)
    extra_low = (extrapolated - extra_high.astype(jnp.float32)).astype(jnp.bfloat16)
    local_total = jnp.sum(extra_high.astype(jnp.float32) + extra_low.astype(jnp.float32), axis=1)
    bus_total = lax.psum(local_total, "col")
    balance_new = balance_dual + (bus_total - demand) / BUSES

    lines_dev = ptdf.shape[0]
    line_devs = lax.axis_size("line")
    first_line = lax.axis_index("line") * lines_dev
    local_line = outage_line - first_line
    inside = (local_line >= 0) & (local_line < lines_dev)
    safe_line = jnp.where(inside, local_line, 0)
    target = jnp.where(inside, local_line, lines_dev)

    rows = injection.shape[0]
    step = rows // CHUNKS
    snapshots = base_dual.shape[0]
    base_rows = base_dual.reshape(line_devs, rows, lines_dev)
    post_rows = post_dual.reshape(line_devs, rows, lines_dev)
    parts = [slice(c * step, (c + 1) * step) for c in range(CHUNKS)]
    new_parts, base_parts, post_parts = pipeline(
        [extra_high[p] for p in parts],
        [extra_low[p] for p in parts],
        [injection[p] for p in parts],
        bus_cost,
        bus_cap,
        [balance_new[p] for p in parts],
        [base_rows[:, p].reshape(line_devs * step, lines_dev) for p in parts],
        [post_rows[:, p].reshape(line_devs * step, lines_dev) for p in parts],
        flow_limit,
        emergency_limit,
        ptdf,
        lodf,
        inside,
        safe_line,
        target,
        outage_weight,
    )
    new_injection = jnp.concatenate(new_parts, axis=0)
    base_new = jnp.stack([b.reshape(line_devs, step, lines_dev) for b in base_parts], axis=1).reshape(snapshots, lines_dev)
    post_new = jnp.stack([b.reshape(line_devs, step, lines_dev) for b in post_parts], axis=1).reshape(snapshots, lines_dev)
    return (new_injection, balance_new, base_new, post_new)


def solution(mesh):
    in_specs = (
        P("line", "col"),
        P("line", "col"),
        P("line", "col"),
        P("line", "col"),
        P("col"),
        P("col"),
        P("line"),
        P("line"),
        P(None, "line"),
        P(None, "line"),
        P("line"),
        P("line"),
        P("col"),
        P("col"),
    )
    out_specs = (P("line", "col"), P("line"), P(None, "line"), P(None, "line"))
    return jax.shard_map(
        on_device, mesh=mesh, in_specs=in_specs, out_specs=out_specs, check_vma=False
    )
```

```python
import jax
import jax.numpy as jnp
from jax import lax
from jax.sharding import PartitionSpec as P

BUSES = 36864


dual_step = 0.5
primal_step = 0.5


def summed_block(value, axis):
    n = lax.axis_size(axis)
    rows = value.shape[0] // n
    parts = lax.all_to_all(value.reshape(n, rows, *value.shape[1:]), axis, 0, 0, tiled=True)
    return parts.sum(axis=0, dtype=value.dtype)


def gathered_rows(block, axis):
    n = lax.axis_size(axis)
    copies = jnp.broadcast_to(block[None], (n, *block.shape))
    whole = lax.all_to_all(copies, axis, 0, 0, tiled=True)
    return whole.reshape(n * block.shape[0], *block.shape[1:])


def full_sum(value, axis):
    return gathered_rows(summed_block(value, axis), axis)


def dual_update(dual, flow, limit):
    shifted = dual + dual_step * flow
    return shifted - dual_step * jnp.clip(shifted / dual_step, -limit, limit)


def on_device(
    ptdf,
    lodf,
    injection,
    injection_prev,
    bus_cost,
    bus_cap,
    demand,
    balance_dual,
    base_dual,
    post_dual,
    flow_limit,
    emergency_limit,
    outage_line,
    outage_weight,
):
    extrapolated = 2.0 * injection - injection_prev
    extra_high = extrapolated.astype(jnp.bfloat16)
    extra_low = (extrapolated - extra_high.astype(jnp.float32)).astype(jnp.bfloat16)
    stacked = jnp.stack([extra_high, extra_low], axis=0)
    lines_dev = ptdf.shape[0]
    ptdf_turned = ptdf.T
    portion = lax.all_gather(stacked, "line", axis=1, tiled=True)
    count = portion.shape[1]
    flat = portion.reshape(2 * count, portion.shape[2])
    product = jnp.dot(flat, ptdf_turned, preferred_element_type=jnp.float32)
    flow_part = product[:count] + product[count:]
    local_total = jnp.sum(extra_high.astype(jnp.float32) + extra_low.astype(jnp.float32), axis=1)
    bus_total = lax.psum(local_total, "col")
    base_flow = full_sum(flow_part, "col")
    balance_new = balance_dual + (bus_total - demand) / BUSES
    base_new = dual_update(base_dual, base_flow, flow_limit[None, :])
    first_line = lax.axis_index("line") * lines_dev
    local_line = outage_line - first_line
    inside = (local_line >= 0) & (local_line < lines_dev)
    safe_line = jnp.where(inside, local_line, 0)
    picked = jnp.take(base_flow, safe_line, axis=1)
    weighted = jnp.where(inside[None, :], picked * outage_weight[None, :], 0.0)
    outage_flow = full_sum(weighted.astype(jnp.bfloat16), "line")
    shift_part = jnp.dot(outage_flow, lodf.T, preferred_element_type=jnp.float32)
    post_shift = full_sum(shift_part, "col")
    post_flow = base_flow + post_shift
    post_new = dual_update(post_dual, post_flow, emergency_limit[None, :])
    back_part = jnp.dot(post_new.astype(jnp.bfloat16), lodf, preferred_element_type=jnp.float32)
    back_flow = full_sum(back_part, "line")
    target = jnp.where(inside, local_line, lines_dev)
    returned_part = (
        jnp.zeros(base_new.shape, jnp.float32)
        .at[:, target]
        .add(back_flow * outage_weight[None, :], mode="drop")
    )
    returned = full_sum(returned_part, "col")
    line_total = (base_new + post_new + returned).astype(jnp.bfloat16)
    prices = lax.psum_scatter(
        jnp.dot(line_total, ptdf, preferred_element_type=jnp.float32),
        "line",
        scatter_dimension=0,
        tiled=True,
    )
    moved = injection - primal_step * (bus_cost[None, :] + prices + balance_new[:, None])
    new_injection = jnp.clip(moved, 0.0, bus_cap[None, :])
    return (new_injection, balance_new, base_new, post_new)


def solution(mesh):
    in_specs = (
        P("line", "col"),
        P("line", "col"),
        P("line", "col"),
        P("line", "col"),
        P("col"),
        P("col"),
        P("line"),
        P("line"),
        P(None, "line"),
        P(None, "line"),
        P("line"),
        P("line"),
        P("col"),
        P("col"),
    )
    out_specs = (P("line", "col"), P("line"), P(None, "line"), P(None, "line"))
    return jax.shard_map(
        on_device, mesh=mesh, in_specs=in_specs, out_specs=out_specs, check_vma=False
    )
```

```python
import jax
import jax.numpy as jnp
from jax import lax
from jax.sharding import PartitionSpec as P

BUSES = 36864


dual_step = 0.5
primal_step = 0.5


def summed_block(value, axis):
    n = lax.axis_size(axis)
    rows = value.shape[0] // n
    parts = lax.all_to_all(value.reshape(n, rows, *value.shape[1:]), axis, 0, 0, tiled=True)
    return parts.sum(axis=0, dtype=value.dtype)


def gathered_rows(block, axis):
    n = lax.axis_size(axis)
    copies = jnp.broadcast_to(block[None], (n, *block.shape))
    whole = lax.all_to_all(copies, axis, 0, 0, tiled=True)
    return whole.reshape(n * block.shape[0], *block.shape[1:])


def full_sum(value, axis):
    return gathered_rows(summed_block(value, axis), axis)


def dual_update(dual, flow, limit):
    shifted = dual + dual_step * flow
    return shifted - dual_step * jnp.clip(shifted / dual_step, -limit, limit)


def on_device(
    ptdf,
    lodf,
    injection,
    injection_prev,
    bus_cost,
    bus_cap,
    demand,
    balance_dual,
    base_dual,
    post_dual,
    flow_limit,
    emergency_limit,
    outage_line,
    outage_weight,
):
    extrapolated = 2.0 * injection - injection_prev
    extra_high = extrapolated.astype(jnp.bfloat16)
    extra_low = (extrapolated - extra_high.astype(jnp.float32)).astype(jnp.bfloat16)
    stacked = jnp.stack([extra_high, extra_low], axis=0)
    lines_dev = ptdf.shape[0]
    ptdf_turned = ptdf.T
    portion = lax.all_gather(stacked, "line", axis=1, tiled=True)
    count = portion.shape[1]
    flat = portion.reshape(2 * count, portion.shape[2])
    product = jnp.dot(flat, ptdf_turned, preferred_element_type=jnp.float32)
    flow_part = product[:count] + product[count:]
    local_total = jnp.sum(extra_high.astype(jnp.float32) + extra_low.astype(jnp.float32), axis=1)
    bus_total = lax.psum(local_total, "col")
    base_flow = full_sum(flow_part, "col")
    balance_new = balance_dual + (bus_total - demand) / BUSES
    base_new = dual_update(base_dual, base_flow, flow_limit[None, :])
    first_line = lax.axis_index("line") * lines_dev
    local_line = outage_line - first_line
    inside = (local_line >= 0) & (local_line < lines_dev)
    safe_line = jnp.where(inside, local_line, 0)
    picked = jnp.take(base_flow, safe_line, axis=1)
    weighted = jnp.where(inside[None, :], picked * outage_weight[None, :], 0.0)
    outage_flow = full_sum(weighted.astype(jnp.bfloat16), "line")
    shift_part = jnp.dot(outage_flow, lodf.T, preferred_element_type=jnp.float32)
    post_shift = full_sum(shift_part, "col")
    post_flow = base_flow + post_shift
    post_new = dual_update(post_dual, post_flow, emergency_limit[None, :])
    back_part = jnp.dot(post_new.astype(jnp.bfloat16), lodf, preferred_element_type=jnp.float32)
    back_flow = full_sum(back_part, "line")
    target = jnp.where(inside, local_line, lines_dev)
    returned_part = (
        jnp.zeros(base_new.shape, jnp.float32)
        .at[:, target]
        .add(back_flow * outage_weight[None, :], mode="drop")
    )
    returned = full_sum(returned_part, "col")
    line_total = (base_new + post_new + returned).astype(jnp.bfloat16)
    split = ptdf.shape[1] // 2
    price_part = jnp.dot(line_total, ptdf, preferred_element_type=jnp.float32)
    prices = jnp.concatenate(
        [
            lax.psum_scatter(price_part[:, :split], "line", scatter_dimension=0, tiled=True),
            summed_block(price_part[:, split:], "line"),
        ],
        axis=1,
    )
    moved = injection - primal_step * (bus_cost[None, :] + prices + balance_new[:, None])
    new_injection = jnp.clip(moved, 0.0, bus_cap[None, :])
    return (new_injection, balance_new, base_new, post_new)


def solution(mesh):
    in_specs = (
        P("line", "col"),
        P("line", "col"),
        P("line", "col"),
        P("line", "col"),
        P("col"),
        P("col"),
        P("line"),
        P("line"),
        P(None, "line"),
        P(None, "line"),
        P("line"),
        P("line"),
        P("col"),
        P("col"),
    )
    out_specs = (P("line", "col"), P("line"), P(None, "line"), P(None, "line"))
    return jax.shard_map(
        on_device, mesh=mesh, in_specs=in_specs, out_specs=out_specs, check_vma=False
    )
```

```python
import jax
import jax.numpy as jnp
from jax import lax
from jax.sharding import Mesh, PartitionSpec as P

BUSES = 36864


dual_step = 0.5
primal_step = 0.5


def summed_block(value, axis):
    n = lax.axis_size(axis)
    rows = value.shape[0] // n
    parts = lax.all_to_all(value.reshape(n, rows, *value.shape[1:]), axis, 0, 0, tiled=True)
    return parts.sum(axis=0, dtype=value.dtype)


def gathered_rows(block, axis):
    n = lax.axis_size(axis)
    copies = jnp.broadcast_to(block[None], (n, *block.shape))
    whole = lax.all_to_all(copies, axis, 0, 0, tiled=True)
    return whole.reshape(n * block.shape[0], *block.shape[1:])


def full_sum(value, axis):
    return gathered_rows(summed_block(value, axis), axis)


LINE_OUTER = "line_outer"
LINE_CORE = "line_core"
LINE = (LINE_OUTER, LINE_CORE)


def swap_cores(value):
    return lax.ppermute(value, LINE_CORE, [(0, 1), (1, 0)])


def line_summed_block(value):
    outer = lax.axis_size(LINE_OUTER)
    core = lax.axis_index(LINE_CORE)
    rows = value.shape[0] // (2 * outer)
    split = value.reshape(outer, 2, rows, *value.shape[1:])
    first, second = split[:, 0], split[:, 1]
    keep = jnp.where(core == 0, first, second)
    give = jnp.where(core == 0, second, first)
    pair_sum = keep + swap_cores(give)
    parts = lax.all_to_all(pair_sum, LINE_OUTER, 0, 0, tiled=True)
    return parts.sum(axis=0, dtype=value.dtype)


def line_gathered_rows(block):
    outer = lax.axis_size(LINE_OUTER)
    core = lax.axis_index(LINE_CORE)
    copies = jnp.broadcast_to(block[None], (outer, *block.shape))
    mine = lax.all_to_all(copies, LINE_OUTER, 0, 0, tiled=True)
    other = swap_cores(mine)
    whole = jnp.where(core == 0, jnp.stack([mine, other], axis=1), jnp.stack([other, mine], axis=1))
    return whole.reshape(2 * outer * block.shape[0], *block.shape[1:])


def line_full_sum(value):
    return line_gathered_rows(line_summed_block(value))


def dual_update(dual, flow, limit):
    shifted = dual + dual_step * flow
    return shifted - dual_step * jnp.clip(shifted / dual_step, -limit, limit)


def on_device(
    ptdf,
    lodf,
    injection,
    injection_prev,
    bus_cost,
    bus_cap,
    demand,
    balance_dual,
    base_dual,
    post_dual,
    flow_limit,
    emergency_limit,
    outage_line,
    outage_weight,
):
    extrapolated = 2.0 * injection - injection_prev
    extra_high = extrapolated.astype(jnp.bfloat16)
    extra_low = (extrapolated - extra_high.astype(jnp.float32)).astype(jnp.bfloat16)
    stacked = jnp.stack([extra_high, extra_low], axis=0)
    lines_dev = ptdf.shape[0]
    ptdf_turned = ptdf.T
    portion = lax.all_gather(stacked, LINE, axis=1, tiled=True)
    count = portion.shape[1]
    flat = portion.reshape(2 * count, portion.shape[2])
    product = jnp.dot(flat, ptdf_turned, preferred_element_type=jnp.float32)
    flow_part = product[:count] + product[count:]
    local_total = jnp.sum(extra_high.astype(jnp.float32) + extra_low.astype(jnp.float32), axis=1)
    bus_total = lax.psum(local_total, "col")
    base_flow = full_sum(flow_part, "col")
    balance_new = balance_dual + (bus_total - demand) / BUSES
    base_new = dual_update(base_dual, base_flow, flow_limit[None, :])
    first_line = lax.axis_index(LINE) * lines_dev
    local_line = outage_line - first_line
    inside = (local_line >= 0) & (local_line < lines_dev)
    safe_line = jnp.where(inside, local_line, 0)
    picked = jnp.take(base_flow, safe_line, axis=1)
    weighted = jnp.where(inside[None, :], picked * outage_weight[None, :], 0.0)
    outage_flow = line_full_sum(weighted.astype(jnp.bfloat16))
    shift_part = jnp.dot(outage_flow, lodf.T, preferred_element_type=jnp.float32)
    post_shift = full_sum(shift_part, "col")
    post_flow = base_flow + post_shift
    post_new = dual_update(post_dual, post_flow, emergency_limit[None, :])
    back_part = jnp.dot(post_new.astype(jnp.bfloat16), lodf, preferred_element_type=jnp.float32)
    back_flow = line_full_sum(back_part)
    target = jnp.where(inside, local_line, lines_dev)
    returned_part = (
        jnp.zeros(base_new.shape, jnp.float32)
        .at[:, target]
        .add(back_flow * outage_weight[None, :], mode="drop")
    )
    returned = full_sum(returned_part, "col")
    line_total = (base_new + post_new + returned).astype(jnp.bfloat16)
    prices = line_summed_block(jnp.dot(line_total, ptdf, preferred_element_type=jnp.float32))
    moved = injection - primal_step * (bus_cost[None, :] + prices + balance_new[:, None])
    new_injection = jnp.clip(moved, 0.0, bus_cap[None, :])
    return (new_injection, balance_new, base_new, post_new)


def solution(mesh):
    outer = mesh.shape["line"] // 2
    fine = Mesh(
        mesh.devices.reshape(outer, 2, mesh.shape["col"]), (LINE_OUTER, LINE_CORE, "col")
    )
    in_specs = (
        P(LINE, "col"),
        P(LINE, "col"),
        P(LINE, "col"),
        P(LINE, "col"),
        P("col"),
        P("col"),
        P(LINE),
        P(LINE),
        P(None, LINE),
        P(None, LINE),
        P(LINE),
        P(LINE),
        P("col"),
        P("col"),
    )
    out_specs = (P(LINE, "col"), P(LINE), P(None, LINE), P(None, LINE))
    return jax.shard_map(
        on_device, mesh=fine, in_specs=in_specs, out_specs=out_specs, check_vma=False
    )
```

```python
import jax
import jax.numpy as jnp
from jax import lax
from jax.sharding import Mesh, PartitionSpec as P

BUSES = 36864


dual_step = 0.5
primal_step = 0.5


def summed_block(value, axis):
    n = lax.axis_size(axis)
    rows = value.shape[0] // n
    parts = lax.all_to_all(value.reshape(n, rows, *value.shape[1:]), axis, 0, 0, tiled=True)
    return parts.sum(axis=0, dtype=value.dtype)


def gathered_rows(block, axis):
    n = lax.axis_size(axis)
    copies = jnp.broadcast_to(block[None], (n, *block.shape))
    whole = lax.all_to_all(copies, axis, 0, 0, tiled=True)
    return whole.reshape(n * block.shape[0], *block.shape[1:])


def full_sum(value, axis):
    return gathered_rows(summed_block(value, axis), axis)


LINE_OUTER = "line_outer"
LINE_CORE = "line_core"
LINE = (LINE_OUTER, LINE_CORE)


def swap_cores(value):
    return lax.ppermute(value, LINE_CORE, [(0, 1), (1, 0)])


def line_summed_block(value):
    outer = lax.axis_size(LINE_OUTER)
    core = lax.axis_index(LINE_CORE)
    rows = value.shape[0] // (2 * outer)
    split = value.reshape(outer, 2, rows, *value.shape[1:])
    first, second = split[:, 0], split[:, 1]
    keep = jnp.where(core == 0, first, second)
    give = jnp.where(core == 0, second, first)
    pair_sum = keep + swap_cores(give)
    parts = lax.all_to_all(pair_sum, LINE_OUTER, 0, 0, tiled=True)
    return parts.sum(axis=0, dtype=value.dtype)


def line_gathered_rows(block):
    outer = lax.axis_size(LINE_OUTER)
    core = lax.axis_index(LINE_CORE)
    copies = jnp.broadcast_to(block[None], (outer, *block.shape))
    mine = lax.all_to_all(copies, LINE_OUTER, 0, 0, tiled=True)
    other = swap_cores(mine)
    whole = jnp.where(core == 0, jnp.stack([mine, other], axis=1), jnp.stack([other, mine], axis=1))
    return whole.reshape(2 * outer * block.shape[0], *block.shape[1:])


def line_full_sum(value):
    return line_gathered_rows(line_summed_block(value))


def dual_update(dual, flow, limit):
    shifted = dual + dual_step * flow
    return shifted - dual_step * jnp.clip(shifted / dual_step, -limit, limit)


def on_device(
    ptdf,
    lodf,
    injection,
    injection_prev,
    bus_cost,
    bus_cap,
    demand,
    balance_dual,
    base_dual,
    post_dual,
    flow_limit,
    emergency_limit,
    outage_line,
    outage_weight,
):
    extrapolated = 2.0 * injection - injection_prev
    extra_high = extrapolated.astype(jnp.bfloat16)
    extra_low = (extrapolated - extra_high.astype(jnp.float32)).astype(jnp.bfloat16)
    stacked = jnp.stack([extra_high, extra_low], axis=0)
    lines_dev = ptdf.shape[0]
    ptdf_turned = ptdf.T
    local_total = jnp.sum(extra_high.astype(jnp.float32) + extra_low.astype(jnp.float32), axis=1)
    bus_total = lax.psum(local_total, "col")
    portion = lax.all_gather(stacked, LINE, axis=1, tiled=True)
    portion, bus_total = lax.optimization_barrier((portion, bus_total))
    count = portion.shape[1]
    flat = portion.reshape(2 * count, portion.shape[2])
    product = jnp.dot(flat, ptdf_turned, preferred_element_type=jnp.float32)
    flow_part = product[:count] + product[count:]
    base_flow = full_sum(flow_part, "col")
    balance_new = balance_dual + (bus_total - demand) / BUSES
    base_new = dual_update(base_dual, base_flow, flow_limit[None, :])
    first_line = lax.axis_index(LINE) * lines_dev
    local_line = outage_line - first_line
    inside = (local_line >= 0) & (local_line < lines_dev)
    safe_line = jnp.where(inside, local_line, 0)
    picked = jnp.take(base_flow, safe_line, axis=1)
    weighted = jnp.where(inside[None, :], picked * outage_weight[None, :], 0.0)
    outage_flow = line_full_sum(weighted.astype(jnp.bfloat16))
    shift_part = jnp.dot(outage_flow, lodf.T, preferred_element_type=jnp.float32)
    post_shift = full_sum(shift_part, "col")
    post_flow = base_flow + post_shift
    post_new = dual_update(post_dual, post_flow, emergency_limit[None, :])
    back_part = jnp.dot(post_new.astype(jnp.bfloat16), lodf, preferred_element_type=jnp.float32)
    back_flow = line_full_sum(back_part)
    target = jnp.where(inside, local_line, lines_dev)
    returned_part = (
        jnp.zeros(base_new.shape, jnp.float32)
        .at[:, target]
        .add(back_flow * outage_weight[None, :], mode="drop")
    )
    returned = full_sum(returned_part, "col")
    line_total = (base_new + post_new + returned).astype(jnp.bfloat16)
    prices = line_summed_block(jnp.dot(line_total, ptdf, preferred_element_type=jnp.float32))
    moved = injection - primal_step * (bus_cost[None, :] + prices + balance_new[:, None])
    new_injection = jnp.clip(moved, 0.0, bus_cap[None, :])
    return (new_injection, balance_new, base_new, post_new)


def solution(mesh):
    outer = mesh.shape["line"] // 2
    fine = Mesh(
        mesh.devices.reshape(outer, 2, mesh.shape["col"]), (LINE_OUTER, LINE_CORE, "col")
    )
    in_specs = (
        P(LINE, "col"),
        P(LINE, "col"),
        P(LINE, "col"),
        P(LINE, "col"),
        P("col"),
        P("col"),
        P(LINE),
        P(LINE),
        P(None, LINE),
        P(None, LINE),
        P(LINE),
        P(LINE),
        P("col"),
        P("col"),
    )
    out_specs = (P(LINE, "col"), P(LINE), P(None, LINE), P(None, LINE))
    return jax.shard_map(
        on_device, mesh=fine, in_specs=in_specs, out_specs=out_specs, check_vma=False
    )
```

```python
import jax
import jax.numpy as jnp
from jax import lax
from jax.sharding import Mesh, PartitionSpec as P

BUSES = 36864


dual_step = 0.5
primal_step = 0.5


def summed_block(value, axis):
    n = lax.axis_size(axis)
    rows = value.shape[0] // n
    parts = lax.all_to_all(value.reshape(n, rows, *value.shape[1:]), axis, 0, 0, tiled=True)
    return parts.sum(axis=0, dtype=value.dtype)


def gathered_rows(block, axis):
    n = lax.axis_size(axis)
    copies = jnp.broadcast_to(block[None], (n, *block.shape))
    whole = lax.all_to_all(copies, axis, 0, 0, tiled=True)
    return whole.reshape(n * block.shape[0], *block.shape[1:])


def full_sum(value, axis):
    return gathered_rows(summed_block(value, axis), axis)


LINE_OUTER = "line_outer"
LINE_CORE = "line_core"
LINE = (LINE_OUTER, LINE_CORE)


def swap_cores(value):
    return lax.ppermute(value, LINE_CORE, [(0, 1), (1, 0)])


def line_summed_block(value):
    outer = lax.axis_size(LINE_OUTER)
    core = lax.axis_index(LINE_CORE)
    rows = value.shape[0] // (2 * outer)
    split = value.reshape(outer, 2, rows, *value.shape[1:])
    first, second = split[:, 0], split[:, 1]
    keep = jnp.where(core == 0, first, second)
    give = jnp.where(core == 0, second, first)
    pair_sum = keep + swap_cores(give)
    parts = lax.all_to_all(pair_sum, LINE_OUTER, 0, 0, tiled=True)
    return parts.sum(axis=0, dtype=value.dtype)


def line_gathered_rows(block):
    outer = lax.axis_size(LINE_OUTER)
    core = lax.axis_index(LINE_CORE)
    copies = jnp.broadcast_to(block[None], (outer, *block.shape))
    mine = lax.all_to_all(copies, LINE_OUTER, 0, 0, tiled=True)
    other = swap_cores(mine)
    whole = jnp.where(core == 0, jnp.stack([mine, other], axis=1), jnp.stack([other, mine], axis=1))
    return whole.reshape(2 * outer * block.shape[0], *block.shape[1:])


def line_full_sum(value):
    return line_gathered_rows(line_summed_block(value))


def split_three(value):
    high = value.astype(jnp.bfloat16)
    rest = value - high.astype(jnp.float32)
    middle = rest.astype(jnp.bfloat16)
    low = (rest - middle.astype(jnp.float32)).astype(jnp.bfloat16)
    return jnp.concatenate([high, middle, low], axis=0)


def add_three(value):
    rows = value.shape[0] // 3
    return value[:rows] + value[rows : 2 * rows] + value[2 * rows :]


def dual_update(dual, flow, limit):
    shifted = dual + dual_step * flow
    return shifted - dual_step * jnp.clip(shifted / dual_step, -limit, limit)


def on_device(
    ptdf,
    lodf,
    injection,
    injection_prev,
    bus_cost,
    bus_cap,
    demand,
    balance_dual,
    base_dual,
    post_dual,
    flow_limit,
    emergency_limit,
    outage_line,
    outage_weight,
):
    extrapolated = 2.0 * injection - injection_prev
    extra_high = extrapolated.astype(jnp.bfloat16)
    extra_low = (extrapolated - extra_high.astype(jnp.float32)).astype(jnp.bfloat16)
    stacked = jnp.stack([extra_high, extra_low], axis=0)
    lines_dev = ptdf.shape[0]
    ptdf_turned = ptdf.T
    local_total = jnp.sum(extra_high.astype(jnp.float32) + extra_low.astype(jnp.float32), axis=1)
    bus_total = lax.psum(local_total, "col")
    portion = lax.all_gather(stacked, LINE, axis=1, tiled=True)
    portion, bus_total = lax.optimization_barrier((portion, bus_total))
    count = portion.shape[1]
    flat = portion.reshape(2 * count, portion.shape[2])
    product = jnp.dot(flat, ptdf_turned, preferred_element_type=jnp.float32)
    flow_part = product[:count] + product[count:]
    base_flow = full_sum(flow_part, "col")
    balance_new = balance_dual + (bus_total - demand) / BUSES
    base_new = dual_update(base_dual, base_flow, flow_limit[None, :])
    first_line = lax.axis_index(LINE) * lines_dev
    local_line = outage_line - first_line
    inside = (local_line >= 0) & (local_line < lines_dev)
    lines_seen = lax.broadcasted_iota(jnp.int32, (lines_dev, outage_line.shape[0]), 0)
    chosen = (lines_seen == local_line[None, :]).astype(jnp.bfloat16)
    picked = add_three(jnp.dot(split_three(base_flow), chosen, preferred_element_type=jnp.float32))
    weighted = jnp.where(inside[None, :], picked * outage_weight[None, :], 0.0)
    outage_flow = line_full_sum(weighted.astype(jnp.bfloat16))
    shift_part = jnp.dot(outage_flow, lodf.T, preferred_element_type=jnp.float32)
    post_shift = full_sum(shift_part, "col")
    post_flow = base_flow + post_shift
    post_new = dual_update(post_dual, post_flow, emergency_limit[None, :])
    back_part = jnp.dot(post_new.astype(jnp.bfloat16), lodf, preferred_element_type=jnp.float32)
    back_flow = line_full_sum(back_part)
    returned_part = add_three(
        lax.dot_general(
            split_three(back_flow * outage_weight[None, :]),
            chosen,
            (((1,), (1,)), ((), ())),
            preferred_element_type=jnp.float32,
        )
    )
    returned = full_sum(returned_part, "col")
    line_total = (base_new + post_new + returned).astype(jnp.bfloat16)
    prices = line_summed_block(jnp.dot(line_total, ptdf, preferred_element_type=jnp.float32))
    moved = injection - primal_step * (bus_cost[None, :] + prices + balance_new[:, None])
    new_injection = jnp.clip(moved, 0.0, bus_cap[None, :])
    return (new_injection, balance_new, base_new, post_new)


def solution(mesh):
    outer = mesh.shape["line"] // 2
    fine = Mesh(
        mesh.devices.reshape(outer, 2, mesh.shape["col"]), (LINE_OUTER, LINE_CORE, "col")
    )
    in_specs = (
        P(LINE, "col"),
        P(LINE, "col"),
        P(LINE, "col"),
        P(LINE, "col"),
        P("col"),
        P("col"),
        P(LINE),
        P(LINE),
        P(None, LINE),
        P(None, LINE),
        P(LINE),
        P(LINE),
        P("col"),
        P("col"),
    )
    out_specs = (P(LINE, "col"), P(LINE), P(None, LINE), P(None, LINE))
    return jax.shard_map(
        on_device, mesh=fine, in_specs=in_specs, out_specs=out_specs, check_vma=False
    )
```

```python
import jax
import jax.numpy as jnp
from jax import lax
from jax.sharding import Mesh, PartitionSpec as P

BUSES = 36864


dual_step = 0.5
primal_step = 0.5


def summed_block(value, axis):
    n = lax.axis_size(axis)
    rows = value.shape[0] // n
    parts = lax.all_to_all(value.reshape(n, rows, *value.shape[1:]), axis, 0, 0, tiled=True)
    return parts.sum(axis=0, dtype=value.dtype)


def gathered_rows(block, axis):
    n = lax.axis_size(axis)
    copies = jnp.broadcast_to(block[None], (n, *block.shape))
    whole = lax.all_to_all(copies, axis, 0, 0, tiled=True)
    return whole.reshape(n * block.shape[0], *block.shape[1:])


def full_sum(value, axis):
    return gathered_rows(summed_block(value, axis), axis)


LINE_OUTER = "line_outer"
LINE_CORE = "line_core"
LINE = (LINE_OUTER, LINE_CORE)


def swap_cores(value):
    return lax.ppermute(value, LINE_CORE, [(0, 1), (1, 0)])


def line_summed_block(value):
    outer = lax.axis_size(LINE_OUTER)
    core = lax.axis_index(LINE_CORE)
    rows = value.shape[0] // (2 * outer)
    split = value.reshape(outer, 2, rows, *value.shape[1:])
    first, second = split[:, 0], split[:, 1]
    keep = jnp.where(core == 0, first, second)
    give = jnp.where(core == 0, second, first)
    pair_sum = keep + swap_cores(give)
    parts = lax.all_to_all(pair_sum, LINE_OUTER, 0, 0, tiled=True)
    return parts.sum(axis=0, dtype=value.dtype)


def line_gathered_rows(block):
    outer = lax.axis_size(LINE_OUTER)
    core = lax.axis_index(LINE_CORE)
    copies = jnp.broadcast_to(block[None], (outer, *block.shape))
    mine = lax.all_to_all(copies, LINE_OUTER, 0, 0, tiled=True)
    other = swap_cores(mine)
    whole = jnp.where(core == 0, jnp.stack([mine, other], axis=1), jnp.stack([other, mine], axis=1))
    return whole.reshape(2 * outer * block.shape[0], *block.shape[1:])


def line_full_sum(value):
    return line_gathered_rows(line_summed_block(value))


def dual_update(dual, flow, limit):
    shifted = dual + dual_step * flow
    return shifted - dual_step * jnp.clip(shifted / dual_step, -limit, limit)


def on_device(
    ptdf,
    lodf,
    injection,
    injection_prev,
    bus_cost,
    bus_cap,
    demand,
    balance_dual,
    base_dual,
    post_dual,
    flow_limit,
    emergency_limit,
    outage_line,
    outage_weight,
):
    extrapolated = 2.0 * injection - injection_prev
    extra_high = extrapolated.astype(jnp.bfloat16)
    extra_low = (extrapolated - extra_high.astype(jnp.float32)).astype(jnp.bfloat16)
    stacked = jnp.stack([extra_high, extra_low], axis=0)
    lines_dev = ptdf.shape[0]
    ptdf_turned = ptdf.T
    local_total = jnp.sum(extra_high.astype(jnp.float32) + extra_low.astype(jnp.float32), axis=1)
    bus_total = lax.psum(local_total, "col")
    portion = lax.all_gather(stacked, LINE, axis=1, tiled=True)
    portion, bus_total = lax.optimization_barrier((portion, bus_total))
    count = portion.shape[1]
    flat = portion.reshape(2 * count, portion.shape[2])
    product = jnp.dot(flat, ptdf_turned, preferred_element_type=jnp.float32)
    flow_part = product[:count] + product[count:]
    base_flow = full_sum(flow_part, "col")
    balance_new = balance_dual + (bus_total - demand) / BUSES
    base_new = dual_update(base_dual, base_flow, flow_limit[None, :])
    first_line = lax.axis_index(LINE) * lines_dev
    local_line = outage_line - first_line
    inside = (local_line >= 0) & (local_line < lines_dev)
    lines_seen = lax.broadcasted_iota(jnp.int32, (lines_dev, outage_line.shape[0]), 0)
    chosen = (lines_seen == local_line[None, :]).astype(jnp.float32)
    exact = lax.Precision.HIGHEST
    picked = jnp.dot(base_flow, chosen, precision=exact, preferred_element_type=jnp.float32)
    weighted = jnp.where(inside[None, :], picked * outage_weight[None, :], 0.0)
    outage_flow = line_full_sum(weighted.astype(jnp.bfloat16))
    shift_part = jnp.dot(outage_flow, lodf.T, preferred_element_type=jnp.float32)
    post_shift = full_sum(shift_part, "col")
    post_flow = base_flow + post_shift
    post_new = dual_update(post_dual, post_flow, emergency_limit[None, :])
    back_part = jnp.dot(post_new.astype(jnp.bfloat16), lodf, preferred_element_type=jnp.float32)
    back_flow = line_full_sum(back_part)
    returned_part = lax.dot_general(
        back_flow * outage_weight[None, :],
        chosen,
        (((1,), (1,)), ((), ())),
        precision=exact,
        preferred_element_type=jnp.float32,
    )
    returned = full_sum(returned_part, "col")
    line_total = (base_new + post_new + returned).astype(jnp.bfloat16)
    prices = line_summed_block(jnp.dot(line_total, ptdf, preferred_element_type=jnp.float32))
    moved = injection - primal_step * (bus_cost[None, :] + prices + balance_new[:, None])
    new_injection = jnp.clip(moved, 0.0, bus_cap[None, :])
    return (new_injection, balance_new, base_new, post_new)


def solution(mesh):
    outer = mesh.shape["line"] // 2
    fine = Mesh(
        mesh.devices.reshape(outer, 2, mesh.shape["col"]), (LINE_OUTER, LINE_CORE, "col")
    )
    in_specs = (
        P(LINE, "col"),
        P(LINE, "col"),
        P(LINE, "col"),
        P(LINE, "col"),
        P("col"),
        P("col"),
        P(LINE),
        P(LINE),
        P(None, LINE),
        P(None, LINE),
        P(LINE),
        P(LINE),
        P("col"),
        P("col"),
    )
    out_specs = (P(LINE, "col"), P(LINE), P(None, LINE), P(None, LINE))
    return jax.shard_map(
        on_device, mesh=fine, in_specs=in_specs, out_specs=out_specs, check_vma=False
    )
```

```python
import jax
import jax.numpy as jnp
from jax import lax
from jax.sharding import Mesh, PartitionSpec as P

BUSES = 36864


dual_step = 0.5
primal_step = 0.5


def summed_block(value, axis):
    n = lax.axis_size(axis)
    rows = value.shape[0] // n
    parts = lax.all_to_all(value.reshape(n, rows, *value.shape[1:]), axis, 0, 0, tiled=True)
    return parts.sum(axis=0, dtype=value.dtype)


def gathered_rows(block, axis):
    n = lax.axis_size(axis)
    copies = jnp.broadcast_to(block[None], (n, *block.shape))
    whole = lax.all_to_all(copies, axis, 0, 0, tiled=True)
    return whole.reshape(n * block.shape[0], *block.shape[1:])


def full_sum(value, axis):
    return gathered_rows(summed_block(value, axis), axis)


LINE_OUTER = "line_outer"
LINE_CORE = "line_core"
LINE = (LINE_OUTER, LINE_CORE)


def swap_cores(value):
    return lax.ppermute(value, LINE_CORE, [(0, 1), (1, 0)])


def line_summed_block(value):
    outer = lax.axis_size(LINE_OUTER)
    core = lax.axis_index(LINE_CORE)
    rows = value.shape[0] // (2 * outer)
    split = value.reshape(outer, 2, rows, *value.shape[1:])
    first, second = split[:, 0], split[:, 1]
    keep = jnp.where(core == 0, first, second)
    give = jnp.where(core == 0, second, first)
    pair_sum = keep + swap_cores(give)
    parts = lax.all_to_all(pair_sum, LINE_OUTER, 0, 0, tiled=True)
    return parts.sum(axis=0, dtype=value.dtype)


def line_gathered_rows(block):
    outer = lax.axis_size(LINE_OUTER)
    core = lax.axis_index(LINE_CORE)
    copies = jnp.broadcast_to(block[None], (outer, *block.shape))
    mine = lax.all_to_all(copies, LINE_OUTER, 0, 0, tiled=True)
    other = swap_cores(mine)
    whole = jnp.where(core == 0, jnp.stack([mine, other], axis=1), jnp.stack([other, mine], axis=1))
    return whole.reshape(2 * outer * block.shape[0], *block.shape[1:])


def line_full_sum(value):
    return line_gathered_rows(line_summed_block(value))


def dual_update(dual, flow, limit):
    shifted = dual + dual_step * flow
    return shifted - dual_step * jnp.clip(shifted / dual_step, -limit, limit)


def on_device(
    ptdf,
    lodf,
    injection,
    injection_prev,
    bus_cost,
    bus_cap,
    demand,
    balance_dual,
    base_dual,
    post_dual,
    flow_limit,
    emergency_limit,
    outage_line,
    outage_weight,
):
    extrapolated = 2.0 * injection - injection_prev
    extra_high = extrapolated.astype(jnp.bfloat16)
    extra_low = (extrapolated - extra_high.astype(jnp.float32)).astype(jnp.bfloat16)
    stacked = jnp.stack([extra_high, extra_low], axis=0)
    lines_dev = ptdf.shape[0]
    ptdf_turned = ptdf.T
    local_total = jnp.sum(extra_high.astype(jnp.float32) + extra_low.astype(jnp.float32), axis=1)
    bus_total = lax.psum(local_total, "col")
    mine = lax.all_gather(stacked, LINE_OUTER, axis=1, tiled=True)
    mine, bus_total = lax.optimization_barrier((mine, bus_total))
    other = swap_cores(mine)
    outer = lax.axis_size(LINE_OUTER)
    rows = injection.shape[0]

    def flows(portion):
        count = portion.shape[1]
        product = jnp.dot(portion.reshape(2 * count, portion.shape[2]), ptdf_turned, preferred_element_type=jnp.float32)
        return (product[:count] + product[count:]).reshape(outer, rows, lines_dev)

    mine_flow, other_flow = flows(mine), flows(other)
    core = lax.axis_index(LINE_CORE)
    flow_part = jnp.where(
        core == 0, jnp.stack([mine_flow, other_flow], axis=1), jnp.stack([other_flow, mine_flow], axis=1)
    ).reshape(2 * outer * rows, lines_dev)
    base_flow = full_sum(flow_part, "col")
    balance_new = balance_dual + (bus_total - demand) / BUSES
    base_new = dual_update(base_dual, base_flow, flow_limit[None, :])
    first_line = lax.axis_index(LINE) * lines_dev
    local_line = outage_line - first_line
    inside = (local_line >= 0) & (local_line < lines_dev)
    lines_seen = lax.broadcasted_iota(jnp.int32, (lines_dev, outage_line.shape[0]), 0)
    chosen = (lines_seen == local_line[None, :]).astype(jnp.float32)
    exact = lax.Precision.HIGHEST
    picked = jnp.dot(base_flow, chosen, precision=exact, preferred_element_type=jnp.float32)
    weighted = jnp.where(inside[None, :], picked * outage_weight[None, :], 0.0)
    outage_flow = line_full_sum(weighted.astype(jnp.bfloat16))
    shift_part = jnp.dot(outage_flow, lodf.T, preferred_element_type=jnp.float32)
    post_shift = full_sum(shift_part, "col")
    post_flow = base_flow + post_shift
    post_new = dual_update(post_dual, post_flow, emergency_limit[None, :])
    back_part = jnp.dot(post_new.astype(jnp.bfloat16), lodf, preferred_element_type=jnp.float32)
    back_flow = line_full_sum(back_part)
    returned_part = lax.dot_general(
        back_flow * outage_weight[None, :],
        chosen,
        (((1,), (1,)), ((), ())),
        precision=exact,
        preferred_element_type=jnp.float32,
    )
    returned = full_sum(returned_part, "col")
    line_total = (base_new + post_new + returned).astype(jnp.bfloat16)
    prices = line_summed_block(jnp.dot(line_total, ptdf, preferred_element_type=jnp.float32))
    moved = injection - primal_step * (bus_cost[None, :] + prices + balance_new[:, None])
    new_injection = jnp.clip(moved, 0.0, bus_cap[None, :])
    return (new_injection, balance_new, base_new, post_new)


def solution(mesh):
    outer = mesh.shape["line"] // 2
    fine = Mesh(
        mesh.devices.reshape(outer, 2, mesh.shape["col"]), (LINE_OUTER, LINE_CORE, "col")
    )
    in_specs = (
        P(LINE, "col"),
        P(LINE, "col"),
        P(LINE, "col"),
        P(LINE, "col"),
        P("col"),
        P("col"),
        P(LINE),
        P(LINE),
        P(None, LINE),
        P(None, LINE),
        P(LINE),
        P(LINE),
        P("col"),
        P("col"),
    )
    out_specs = (P(LINE, "col"), P(LINE), P(None, LINE), P(None, LINE))
    return jax.shard_map(
        on_device, mesh=fine, in_specs=in_specs, out_specs=out_specs, check_vma=False
    )
```

```python
import jax
import jax.numpy as jnp
from jax import lax
from jax.sharding import Mesh, PartitionSpec as P

BUSES = 36864


dual_step = 0.5
primal_step = 0.5


def summed_block(value, axis):
    n = lax.axis_size(axis)
    rows = value.shape[0] // n
    parts = lax.all_to_all(value.reshape(n, rows, *value.shape[1:]), axis, 0, 0, tiled=True)
    return parts.sum(axis=0, dtype=value.dtype)


def gathered_rows(block, axis):
    n = lax.axis_size(axis)
    copies = jnp.broadcast_to(block[None], (n, *block.shape))
    whole = lax.all_to_all(copies, axis, 0, 0, tiled=True)
    return whole.reshape(n * block.shape[0], *block.shape[1:])


def full_sum(value, axis):
    return gathered_rows(summed_block(value, axis), axis)


LINE_OUTER = "line_outer"
LINE_CORE = "line_core"
LINE = (LINE_OUTER, LINE_CORE)


def swap_cores(value):
    return lax.ppermute(value, LINE_CORE, [(0, 1), (1, 0)])


def line_summed_block(value):
    outer = lax.axis_size(LINE_OUTER)
    core = lax.axis_index(LINE_CORE)
    rows = value.shape[0] // (2 * outer)
    split = value.reshape(outer, 2, rows, *value.shape[1:])
    first, second = split[:, 0], split[:, 1]
    keep = jnp.where(core == 0, first, second)
    give = jnp.where(core == 0, second, first)
    pair_sum = keep + swap_cores(give)
    parts = lax.all_to_all(pair_sum, LINE_OUTER, 0, 0, tiled=True)
    return parts.sum(axis=0, dtype=value.dtype)


def line_gathered_rows(block):
    outer = lax.axis_size(LINE_OUTER)
    core = lax.axis_index(LINE_CORE)
    copies = jnp.broadcast_to(block[None], (outer, *block.shape))
    mine = lax.all_to_all(copies, LINE_OUTER, 0, 0, tiled=True)
    other = swap_cores(mine)
    whole = jnp.where(core == 0, jnp.stack([mine, other], axis=1), jnp.stack([other, mine], axis=1))
    return whole.reshape(2 * outer * block.shape[0], *block.shape[1:])


def line_full_sum(value):
    return line_gathered_rows(line_summed_block(value))


def dual_update(dual, flow, limit):
    shifted = dual + dual_step * flow
    return shifted - dual_step * jnp.clip(shifted / dual_step, -limit, limit)


def on_device(
    ptdf,
    lodf,
    injection,
    injection_prev,
    bus_cost,
    bus_cap,
    demand,
    balance_dual,
    base_dual,
    post_dual,
    flow_limit,
    emergency_limit,
    outage_line,
    outage_weight,
):
    extrapolated = 2.0 * injection - injection_prev
    extra_high = extrapolated.astype(jnp.bfloat16)
    extra_low = (extrapolated - extra_high.astype(jnp.float32)).astype(jnp.bfloat16)
    stacked = jnp.stack([extra_high, extra_low], axis=0)
    lines_dev = ptdf.shape[0]
    ptdf_turned = ptdf.T
    local_total = jnp.sum(extra_high.astype(jnp.float32) + extra_low.astype(jnp.float32), axis=1)
    bus_total = lax.psum(local_total, "col")
    portion = lax.all_gather(stacked, LINE, axis=1, tiled=True)
    portion, bus_total = lax.optimization_barrier((portion, bus_total))
    count = portion.shape[1]
    flat = portion.reshape(2 * count, portion.shape[2])
    product = jnp.dot(flat, ptdf_turned, preferred_element_type=jnp.float32)
    flow_part = product[:count] + product[count:]
    base_flow = full_sum(flow_part, "col")
    balance_new = balance_dual + (bus_total - demand) / BUSES
    base_new = dual_update(base_dual, base_flow, flow_limit[None, :])
    first_line = lax.axis_index(LINE) * lines_dev
    local_line = outage_line - first_line
    inside = (local_line >= 0) & (local_line < lines_dev)
    lines_seen = lax.broadcasted_iota(jnp.int32, (lines_dev, outage_line.shape[0]), 0)
    chosen = (lines_seen == local_line[None, :]).astype(jnp.float32)
    exact = lax.Precision.HIGHEST
    picked = jnp.dot(base_flow, chosen, precision=exact, preferred_element_type=jnp.float32)
    weighted = jnp.where(inside[None, :], picked * outage_weight[None, :], 0.0)
    outage_flow = line_full_sum(weighted.astype(jnp.bfloat16))
    shift_part = jnp.dot(outage_flow, lodf.T, preferred_element_type=jnp.float32)
    post_shift = full_sum(shift_part, "col")
    post_flow = base_flow + post_shift
    post_new = dual_update(post_dual, post_flow, emergency_limit[None, :])
    back_part = jnp.dot(post_new.astype(jnp.bfloat16), lodf, preferred_element_type=jnp.float32)
    back_flow = line_full_sum(back_part)
    returned_part = lax.dot_general(
        back_flow * outage_weight[None, :],
        chosen,
        (((1,), (1,)), ((), ())),
        precision=exact,
        preferred_element_type=jnp.float32,
    )
    returned = summed_block(returned_part, "col")
    block_rows = returned.shape[0]
    first_row = lax.axis_index("col") * block_rows
    base_block = lax.dynamic_slice_in_dim(base_new, first_row, block_rows, axis=0)
    post_block = lax.dynamic_slice_in_dim(post_new, first_row, block_rows, axis=0)
    line_total = gathered_rows((base_block + post_block + returned).astype(jnp.bfloat16), "col")
    prices = line_summed_block(jnp.dot(line_total, ptdf, preferred_element_type=jnp.float32))
    moved = injection - primal_step * (bus_cost[None, :] + prices + balance_new[:, None])
    new_injection = jnp.clip(moved, 0.0, bus_cap[None, :])
    return (new_injection, balance_new, base_new, post_new)


def solution(mesh):
    outer = mesh.shape["line"] // 2
    fine = Mesh(
        mesh.devices.reshape(outer, 2, mesh.shape["col"]), (LINE_OUTER, LINE_CORE, "col")
    )
    in_specs = (
        P(LINE, "col"),
        P(LINE, "col"),
        P(LINE, "col"),
        P(LINE, "col"),
        P("col"),
        P("col"),
        P(LINE),
        P(LINE),
        P(None, LINE),
        P(None, LINE),
        P(LINE),
        P(LINE),
        P("col"),
        P("col"),
    )
    out_specs = (P(LINE, "col"), P(LINE), P(None, LINE), P(None, LINE))
    return jax.shard_map(
        on_device, mesh=fine, in_specs=in_specs, out_specs=out_specs, check_vma=False
    )
```

```python
import jax
import jax.numpy as jnp
from jax import lax
from jax.sharding import Mesh, PartitionSpec as P

BUSES = 36864


dual_step = 0.5
primal_step = 0.5


def summed_block(value, axis):
    n = lax.axis_size(axis)
    rows = value.shape[0] // n
    parts = lax.all_to_all(value.reshape(n, rows, *value.shape[1:]), axis, 0, 0, tiled=True)
    return parts.sum(axis=0, dtype=value.dtype)


def gathered_rows(block, axis):
    n = lax.axis_size(axis)
    copies = jnp.broadcast_to(block[None], (n, *block.shape))
    whole = lax.all_to_all(copies, axis, 0, 0, tiled=True)
    return whole.reshape(n * block.shape[0], *block.shape[1:])


def full_sum(value, axis):
    return gathered_rows(summed_block(value, axis), axis)


LINE_OUTER = "line_outer"
LINE_CORE = "line_core"
LINE = (LINE_OUTER, LINE_CORE)


def swap_cores(value):
    return lax.ppermute(value, LINE_CORE, [(0, 1), (1, 0)])


def line_summed_block(value):
    outer = lax.axis_size(LINE_OUTER)
    core = lax.axis_index(LINE_CORE)
    rows = value.shape[0] // (2 * outer)
    split = value.reshape(outer, 2, rows, *value.shape[1:])
    first, second = split[:, 0], split[:, 1]
    keep = jnp.where(core == 0, first, second)
    give = jnp.where(core == 0, second, first)
    pair_sum = keep + swap_cores(give)
    parts = lax.all_to_all(pair_sum, LINE_OUTER, 0, 0, tiled=True)
    return parts.sum(axis=0, dtype=value.dtype)


def line_gathered_rows(block):
    outer = lax.axis_size(LINE_OUTER)
    core = lax.axis_index(LINE_CORE)
    copies = jnp.broadcast_to(block[None], (outer, *block.shape))
    mine = lax.all_to_all(copies, LINE_OUTER, 0, 0, tiled=True)
    other = swap_cores(mine)
    whole = jnp.where(core == 0, jnp.stack([mine, other], axis=1), jnp.stack([other, mine], axis=1))
    return whole.reshape(2 * outer * block.shape[0], *block.shape[1:])


def line_full_sum(value):
    return line_gathered_rows(line_summed_block(value))


def dual_update(dual, flow, limit):
    shifted = dual + dual_step * flow
    return shifted - dual_step * jnp.clip(shifted / dual_step, -limit, limit)


def on_device(
    ptdf,
    lodf,
    injection,
    injection_prev,
    bus_cost,
    bus_cap,
    demand,
    balance_dual,
    base_dual,
    post_dual,
    flow_limit,
    emergency_limit,
    outage_line,
    outage_weight,
):
    extrapolated = 2.0 * injection - injection_prev
    extra_high = extrapolated.astype(jnp.bfloat16)
    extra_low = (extrapolated - extra_high.astype(jnp.float32)).astype(jnp.bfloat16)
    stacked = jnp.stack([extra_high, extra_low], axis=0)
    lines_dev = ptdf.shape[0]
    ptdf_turned = ptdf.T
    outer = lax.axis_size(LINE_OUTER)
    line_devs = 2 * outer
    rows = injection.shape[0]
    half = rows // 2

    def flows(portion):
        lead = portion.shape[:-3]
        count = portion.shape[-2]
        flat = portion.reshape(-1, portion.shape[-1])
        product = jnp.dot(flat, ptdf_turned, preferred_element_type=jnp.float32)
        product = product.reshape(*lead, 2, count, lines_dev)
        return product[..., 0, :, :] + product[..., 1, :, :]

    by_gather = lax.all_gather(stacked[:, :half], LINE, axis=1, tiled=True)
    copies = jnp.broadcast_to(stacked[None, :, half:], (outer, *stacked[:, half:].shape))
    mine = lax.all_to_all(copies, LINE_OUTER, 0, 0, tiled=True)
    other = swap_cores(mine)
    core = lax.axis_index(LINE_CORE)
    gather_flow = flows(by_gather).reshape(line_devs, half, lines_dev)
    mine_flow, other_flow = flows(mine), flows(other)
    swap_flow = jnp.where(
        core == 0, jnp.stack([mine_flow, other_flow], axis=1), jnp.stack([other_flow, mine_flow], axis=1)
    ).reshape(line_devs, rows - half, lines_dev)
    flow_part = jnp.concatenate([gather_flow, swap_flow], axis=1).reshape(line_devs * rows, lines_dev)
    local_total = jnp.sum(extra_high.astype(jnp.float32) + extra_low.astype(jnp.float32), axis=1)
    first_snapshot = lax.axis_index(LINE) * rows
    totals = lax.dynamic_update_slice(
        jnp.zeros((line_devs * rows, 128), jnp.float32),
        jnp.broadcast_to(local_total[:, None], (rows, 128)),
        (first_snapshot, 0),
    )
    summed = full_sum(jnp.concatenate([flow_part, totals], axis=1), "col")
    base_flow = summed[:, :lines_dev]
    bus_total = lax.dynamic_slice_in_dim(summed[:, lines_dev], first_snapshot, rows)
    balance_new = balance_dual + (bus_total - demand) / BUSES
    base_new = dual_update(base_dual, base_flow, flow_limit[None, :])
    first_line = lax.axis_index(LINE) * lines_dev
    local_line = outage_line - first_line
    inside = (local_line >= 0) & (local_line < lines_dev)
    lines_seen = lax.broadcasted_iota(jnp.int32, (lines_dev, outage_line.shape[0]), 0)
    chosen = (lines_seen == local_line[None, :]).astype(jnp.float32)
    exact = lax.Precision.HIGHEST
    picked = jnp.dot(base_flow, chosen, precision=exact, preferred_element_type=jnp.float32)
    weighted = jnp.where(inside[None, :], picked * outage_weight[None, :], 0.0)
    outage_flow = line_full_sum(weighted.astype(jnp.bfloat16))
    shift_part = jnp.dot(outage_flow, lodf.T, preferred_element_type=jnp.float32)
    post_shift = full_sum(shift_part, "col")
    post_flow = base_flow + post_shift
    post_new = dual_update(post_dual, post_flow, emergency_limit[None, :])
    back_part = jnp.dot(post_new.astype(jnp.bfloat16), lodf, preferred_element_type=jnp.float32)
    back_flow = line_full_sum(back_part)
    returned_part = lax.dot_general(
        back_flow * outage_weight[None, :],
        chosen,
        (((1,), (1,)), ((), ())),
        precision=exact,
        preferred_element_type=jnp.float32,
    )
    returned = summed_block(returned_part, "col")
    block_rows = returned.shape[0]
    first_row = lax.axis_index("col") * block_rows
    base_block = lax.dynamic_slice_in_dim(base_new, first_row, block_rows, axis=0)
    post_block = lax.dynamic_slice_in_dim(post_new, first_row, block_rows, axis=0)
    line_total = gathered_rows((base_block + post_block + returned).astype(jnp.bfloat16), "col")
    prices = line_summed_block(jnp.dot(line_total, ptdf, preferred_element_type=jnp.float32))
    moved = injection - primal_step * (bus_cost[None, :] + prices + balance_new[:, None])
    new_injection = jnp.clip(moved, 0.0, bus_cap[None, :])
    return (new_injection, balance_new, base_new, post_new)


def solution(mesh):
    outer = mesh.shape["line"] // 2
    fine = Mesh(
        mesh.devices.reshape(outer, 2, mesh.shape["col"]), (LINE_OUTER, LINE_CORE, "col")
    )
    in_specs = (
        P(LINE, "col"),
        P(LINE, "col"),
        P(LINE, "col"),
        P(LINE, "col"),
        P("col"),
        P("col"),
        P(LINE),
        P(LINE),
        P(None, LINE),
        P(None, LINE),
        P(LINE),
        P(LINE),
        P("col"),
        P("col"),
    )
    out_specs = (P(LINE, "col"), P(LINE), P(None, LINE), P(None, LINE))
    return jax.shard_map(
        on_device, mesh=fine, in_specs=in_specs, out_specs=out_specs, check_vma=False
    )
```

```python
import jax
import jax.numpy as jnp
from jax import lax
from jax.sharding import Mesh, PartitionSpec as P

BUSES = 36864


dual_step = 0.5
primal_step = 0.5


def summed_block(value, axis):
    n = lax.axis_size(axis)
    rows = value.shape[0] // n
    parts = lax.all_to_all(value.reshape(n, rows, *value.shape[1:]), axis, 0, 0, tiled=True)
    return parts.sum(axis=0, dtype=value.dtype)


def gathered_rows(block, axis):
    n = lax.axis_size(axis)
    copies = jnp.broadcast_to(block[None], (n, *block.shape))
    whole = lax.all_to_all(copies, axis, 0, 0, tiled=True)
    return whole.reshape(n * block.shape[0], *block.shape[1:])


def full_sum(value, axis):
    return gathered_rows(summed_block(value, axis), axis)


LINE_OUTER = "line_outer"
LINE_CORE = "line_core"
LINE = (LINE_OUTER, LINE_CORE)


def swap_cores(value):
    return lax.ppermute(value, LINE_CORE, [(0, 1), (1, 0)])


def line_summed_block(value):
    outer = lax.axis_size(LINE_OUTER)
    core = lax.axis_index(LINE_CORE)
    rows = value.shape[0] // (2 * outer)
    split = value.reshape(outer, 2, rows, *value.shape[1:])
    first, second = split[:, 0], split[:, 1]
    keep = jnp.where(core == 0, first, second)
    give = jnp.where(core == 0, second, first)
    pair_sum = keep + swap_cores(give)
    parts = lax.all_to_all(pair_sum, LINE_OUTER, 0, 0, tiled=True)
    return parts.sum(axis=0, dtype=value.dtype)


def line_gathered_rows(block):
    outer = lax.axis_size(LINE_OUTER)
    core = lax.axis_index(LINE_CORE)
    copies = jnp.broadcast_to(block[None], (outer, *block.shape))
    mine = lax.all_to_all(copies, LINE_OUTER, 0, 0, tiled=True)
    other = swap_cores(mine)
    whole = jnp.where(core == 0, jnp.stack([mine, other], axis=1), jnp.stack([other, mine], axis=1))
    return whole.reshape(2 * outer * block.shape[0], *block.shape[1:])


def line_full_sum(value):
    return line_gathered_rows(line_summed_block(value))


def dual_update(dual, flow, limit):
    shifted = dual + dual_step * flow
    return shifted - dual_step * jnp.clip(shifted / dual_step, -limit, limit)


def on_device(
    ptdf,
    lodf,
    injection,
    injection_prev,
    bus_cost,
    bus_cap,
    demand,
    balance_dual,
    base_dual,
    post_dual,
    flow_limit,
    emergency_limit,
    outage_line,
    outage_weight,
):
    extrapolated = 2.0 * injection - injection_prev
    extra_high = extrapolated.astype(jnp.bfloat16)
    extra_low = (extrapolated - extra_high.astype(jnp.float32)).astype(jnp.bfloat16)
    stacked = jnp.stack([extra_high, extra_low], axis=0)
    lines_dev = ptdf.shape[0]
    ptdf_turned = ptdf.T
    outer = lax.axis_size(LINE_OUTER)
    line_devs = 2 * outer
    rows = injection.shape[0]
    half = rows - rows // 4

    def flows(portion):
        lead = portion.shape[:-3]
        count = portion.shape[-2]
        flat = portion.reshape(-1, portion.shape[-1])
        product = jnp.dot(flat, ptdf_turned, preferred_element_type=jnp.float32)
        product = product.reshape(*lead, 2, count, lines_dev)
        return product[..., 0, :, :] + product[..., 1, :, :]

    local_total = jnp.sum(extra_high.astype(jnp.float32) + extra_low.astype(jnp.float32), axis=1)
    bus_total = lax.psum(local_total, "col")
    by_gather = lax.all_gather(stacked[:, :half], LINE, axis=1, tiled=True)
    by_gather, bus_total = lax.optimization_barrier((by_gather, bus_total))
    copies = jnp.broadcast_to(stacked[None, :, half:], (outer, *stacked[:, half:].shape))
    mine = lax.all_to_all(copies, LINE_OUTER, 0, 0, tiled=True)
    other = swap_cores(mine)
    core = lax.axis_index(LINE_CORE)
    gather_flow = flows(by_gather).reshape(line_devs, half, lines_dev)
    mine_flow, other_flow = flows(mine), flows(other)
    swap_flow = jnp.where(
        core == 0, jnp.stack([mine_flow, other_flow], axis=1), jnp.stack([other_flow, mine_flow], axis=1)
    ).reshape(line_devs, rows - half, lines_dev)
    flow_part = jnp.concatenate([gather_flow, swap_flow], axis=1).reshape(line_devs * rows, lines_dev)
    base_flow = full_sum(flow_part, "col")
    balance_new = balance_dual + (bus_total - demand) / BUSES
    base_new = dual_update(base_dual, base_flow, flow_limit[None, :])
    first_line = lax.axis_index(LINE) * lines_dev
    local_line = outage_line - first_line
    inside = (local_line >= 0) & (local_line < lines_dev)
    lines_seen = lax.broadcasted_iota(jnp.int32, (lines_dev, outage_line.shape[0]), 0)
    chosen = (lines_seen == local_line[None, :]).astype(jnp.float32)
    exact = lax.Precision.HIGHEST
    picked = jnp.dot(base_flow, chosen, precision=exact, preferred_element_type=jnp.float32)
    weighted = jnp.where(inside[None, :], picked * outage_weight[None, :], 0.0)
    outage_flow = line_full_sum(weighted.astype(jnp.bfloat16))
    shift_part = jnp.dot(outage_flow, lodf.T, preferred_element_type=jnp.float32)
    post_shift = full_sum(shift_part, "col")
    post_flow = base_flow + post_shift
    post_new = dual_update(post_dual, post_flow, emergency_limit[None, :])
    back_part = jnp.dot(post_new.astype(jnp.bfloat16), lodf, preferred_element_type=jnp.float32)
    back_flow = line_full_sum(back_part)
    returned_part = lax.dot_general(
        back_flow * outage_weight[None, :],
        chosen,
        (((1,), (1,)), ((), ())),
        precision=exact,
        preferred_element_type=jnp.float32,
    )
    returned = summed_block(returned_part, "col")
    block_rows = returned.shape[0]
    first_row = lax.axis_index("col") * block_rows
    base_block = lax.dynamic_slice_in_dim(base_new, first_row, block_rows, axis=0)
    post_block = lax.dynamic_slice_in_dim(post_new, first_row, block_rows, axis=0)
    line_total = gathered_rows((base_block + post_block + returned).astype(jnp.bfloat16), "col")
    prices = line_summed_block(jnp.dot(line_total, ptdf, preferred_element_type=jnp.float32))
    moved = injection - primal_step * (bus_cost[None, :] + prices + balance_new[:, None])
    new_injection = jnp.clip(moved, 0.0, bus_cap[None, :])
    return (new_injection, balance_new, base_new, post_new)


def solution(mesh):
    outer = mesh.shape["line"] // 2
    fine = Mesh(
        mesh.devices.reshape(outer, 2, mesh.shape["col"]), (LINE_OUTER, LINE_CORE, "col")
    )
    in_specs = (
        P(LINE, "col"),
        P(LINE, "col"),
        P(LINE, "col"),
        P(LINE, "col"),
        P("col"),
        P("col"),
        P(LINE),
        P(LINE),
        P(None, LINE),
        P(None, LINE),
        P(LINE),
        P(LINE),
        P("col"),
        P("col"),
    )
    out_specs = (P(LINE, "col"), P(LINE), P(None, LINE), P(None, LINE))
    return jax.shard_map(
        on_device, mesh=fine, in_specs=in_specs, out_specs=out_specs, check_vma=False
    )
```

```python
import jax
import jax.numpy as jnp
from jax import lax
from jax.sharding import Mesh, PartitionSpec as P

BUSES = 36864


dual_step = 0.5
primal_step = 0.5


def summed_block(value, axis):
    n = lax.axis_size(axis)
    rows = value.shape[0] // n
    parts = lax.all_to_all(value.reshape(n, rows, *value.shape[1:]), axis, 0, 0, tiled=True)
    return parts.sum(axis=0, dtype=value.dtype)


def gathered_rows(block, axis):
    n = lax.axis_size(axis)
    copies = jnp.broadcast_to(block[None], (n, *block.shape))
    whole = lax.all_to_all(copies, axis, 0, 0, tiled=True)
    return whole.reshape(n * block.shape[0], *block.shape[1:])


def full_sum(value, axis):
    return gathered_rows(summed_block(value, axis), axis)


LINE_OUTER = "line_outer"
LINE_CORE = "line_core"
LINE = (LINE_OUTER, LINE_CORE)


def swap_cores(value):
    return lax.ppermute(value, LINE_CORE, [(0, 1), (1, 0)])


def line_summed_block(value):
    outer = lax.axis_size(LINE_OUTER)
    core = lax.axis_index(LINE_CORE)
    rows = value.shape[0] // (2 * outer)
    split = value.reshape(outer, 2, rows, *value.shape[1:])
    first, second = split[:, 0], split[:, 1]
    keep = jnp.where(core == 0, first, second)
    give = jnp.where(core == 0, second, first)
    pair_sum = keep + swap_cores(give)
    parts = lax.all_to_all(pair_sum, LINE_OUTER, 0, 0, tiled=True)
    return parts.sum(axis=0, dtype=value.dtype)


def line_gathered_rows(block):
    outer = lax.axis_size(LINE_OUTER)
    core = lax.axis_index(LINE_CORE)
    copies = jnp.broadcast_to(block[None], (outer, *block.shape))
    mine = lax.all_to_all(copies, LINE_OUTER, 0, 0, tiled=True)
    other = swap_cores(mine)
    whole = jnp.where(core == 0, jnp.stack([mine, other], axis=1), jnp.stack([other, mine], axis=1))
    return whole.reshape(2 * outer * block.shape[0], *block.shape[1:])


def line_full_sum(value):
    return line_gathered_rows(line_summed_block(value))


def dual_update(dual, flow, limit):
    shifted = dual + dual_step * flow
    return shifted - dual_step * jnp.clip(shifted / dual_step, -limit, limit)


def on_device(
    ptdf,
    lodf,
    injection,
    injection_prev,
    bus_cost,
    bus_cap,
    demand,
    balance_dual,
    base_dual,
    post_dual,
    flow_limit,
    emergency_limit,
    outage_line,
    outage_weight,
):
    extrapolated = 2.0 * injection - injection_prev
    extra_high = extrapolated.astype(jnp.bfloat16)
    extra_low = (extrapolated - extra_high.astype(jnp.float32)).astype(jnp.bfloat16)
    stacked = jnp.stack([extra_high, extra_low], axis=0)
    lines_dev = ptdf.shape[0]
    ptdf_turned = ptdf.T
    outer = lax.axis_size(LINE_OUTER)
    line_devs = 2 * outer
    rows = injection.shape[0]
    half = rows - rows // 4

    def flows(portion):
        lead = portion.shape[:-3]
        count = portion.shape[-2]
        flat = portion.reshape(-1, portion.shape[-1])
        product = jnp.dot(flat, ptdf_turned, preferred_element_type=jnp.float32)
        product = product.reshape(*lead, 2, count, lines_dev)
        return product[..., 0, :, :] + product[..., 1, :, :]

    local_total = jnp.sum(extra_high.astype(jnp.float32) + extra_low.astype(jnp.float32), axis=1)
    bus_total = lax.psum(local_total, "col")
    by_gather = lax.all_gather(stacked[:, :half], LINE, axis=1, tiled=True)
    by_gather, bus_total = lax.optimization_barrier((by_gather, bus_total))
    copies = jnp.broadcast_to(stacked[None, :, half:], (outer, *stacked[:, half:].shape))
    mine = lax.all_to_all(copies, LINE_OUTER, 0, 0, tiled=True)
    other = swap_cores(mine)
    core = lax.axis_index(LINE_CORE)
    gather_flow = flows(by_gather).reshape(line_devs, half, lines_dev)
    mine_flow, other_flow = flows(mine), flows(other)
    swap_flow = jnp.where(
        core == 0, jnp.stack([mine_flow, other_flow], axis=1), jnp.stack([other_flow, mine_flow], axis=1)
    ).reshape(line_devs, rows - half, lines_dev)
    flow_part = jnp.concatenate([gather_flow, swap_flow], axis=1).reshape(line_devs * rows, lines_dev)
    base_flow = full_sum(flow_part, "col")
    balance_new = balance_dual + (bus_total - demand) / BUSES
    base_new = dual_update(base_dual, base_flow, flow_limit[None, :])
    first_line = lax.axis_index(LINE) * lines_dev
    local_line = outage_line - first_line
    inside = (local_line >= 0) & (local_line < lines_dev)
    lines_seen = lax.broadcasted_iota(jnp.int32, (lines_dev, outage_line.shape[0]), 0)
    chosen = (lines_seen == local_line[None, :]).astype(jnp.float32)
    exact = lax.Precision.HIGHEST
    picked = jnp.dot(base_flow, chosen, precision=exact, preferred_element_type=jnp.float32)
    weighted = jnp.where(inside[None, :], picked * outage_weight[None, :], 0.0)
    outage_flow = line_full_sum(weighted.astype(jnp.bfloat16))
    shift_part = jnp.dot(outage_flow, lodf.T, preferred_element_type=jnp.float32)
    post_shift = full_sum(shift_part, "col")
    post_flow = base_flow + post_shift
    post_new = dual_update(post_dual, post_flow, emergency_limit[None, :])
    back_part = jnp.dot(post_new.astype(jnp.bfloat16), lodf, preferred_element_type=jnp.float32)
    back_flow = line_full_sum(back_part)
    returned_part = lax.dot_general(
        back_flow * outage_weight[None, :],
        chosen,
        (((1,), (1,)), ((), ())),
        precision=exact,
        preferred_element_type=jnp.float32,
    )
    returned = summed_block(returned_part, "col")
    block_rows = returned.shape[0]
    first_row = lax.axis_index("col") * block_rows
    base_block = lax.dynamic_slice_in_dim(base_new, first_row, block_rows, axis=0)
    post_block = lax.dynamic_slice_in_dim(post_new, first_row, block_rows, axis=0)
    line_total = gathered_rows((base_block + post_block + returned).astype(jnp.bfloat16), "col")
    outer_devs = lax.axis_size(LINE_OUTER)
    core_now = lax.axis_index(LINE_CORE)
    by_core = line_total.reshape(outer_devs, 2, line_total.shape[0] // (2 * outer_devs), line_total.shape[1])
    keep_rows = jnp.where(core_now == 0, by_core[:, 0], by_core[:, 1])
    give_rows = jnp.where(core_now == 0, by_core[:, 1], by_core[:, 0])
    given = swap_cores(jnp.dot(give_rows, ptdf, preferred_element_type=jnp.float32))
    kept = lax.optimization_barrier(jnp.dot(keep_rows, ptdf, preferred_element_type=jnp.float32))
    pair_sum = kept + given
    prices = lax.all_to_all(pair_sum, LINE_OUTER, 0, 0, tiled=True).sum(axis=0, dtype=jnp.float32)
    moved = injection - primal_step * (bus_cost[None, :] + prices + balance_new[:, None])
    new_injection = jnp.clip(moved, 0.0, bus_cap[None, :])
    return (new_injection, balance_new, base_new, post_new)


def solution(mesh):
    outer = mesh.shape["line"] // 2
    fine = Mesh(
        mesh.devices.reshape(outer, 2, mesh.shape["col"]), (LINE_OUTER, LINE_CORE, "col")
    )
    in_specs = (
        P(LINE, "col"),
        P(LINE, "col"),
        P(LINE, "col"),
        P(LINE, "col"),
        P("col"),
        P("col"),
        P(LINE),
        P(LINE),
        P(None, LINE),
        P(None, LINE),
        P(LINE),
        P(LINE),
        P("col"),
        P("col"),
    )
    out_specs = (P(LINE, "col"), P(LINE), P(None, LINE), P(None, LINE))

    return jax.shard_map(on_device, mesh=fine, in_specs=in_specs, out_specs=out_specs, check_vma=False)
```

```python
import jax
import jax.numpy as jnp
from jax import lax
from jax.sharding import Mesh, PartitionSpec as P

BUSES = 36864


dual_step = 0.5
primal_step = 0.5


def summed_block(value, axis):
    n = lax.axis_size(axis)
    rows = value.shape[0] // n
    parts = lax.all_to_all(value.reshape(n, rows, *value.shape[1:]), axis, 0, 0, tiled=True)
    return parts.sum(axis=0, dtype=value.dtype)


def gathered_rows(block, axis):
    n = lax.axis_size(axis)
    copies = jnp.broadcast_to(block[None], (n, *block.shape))
    whole = lax.all_to_all(copies, axis, 0, 0, tiled=True)
    return whole.reshape(n * block.shape[0], *block.shape[1:])


def full_sum(value, axis):
    return gathered_rows(summed_block(value, axis), axis)


LINE_OUTER = "line_outer"
LINE_CORE = "line_core"
LINE = (LINE_OUTER, LINE_CORE)


def swap_cores(value):
    return lax.ppermute(value, LINE_CORE, [(0, 1), (1, 0)])


def line_summed_block(value):
    outer = lax.axis_size(LINE_OUTER)
    core = lax.axis_index(LINE_CORE)
    rows = value.shape[0] // (2 * outer)
    split = value.reshape(outer, 2, rows, *value.shape[1:])
    first, second = split[:, 0], split[:, 1]
    keep = jnp.where(core == 0, first, second)
    give = jnp.where(core == 0, second, first)
    pair_sum = keep + swap_cores(give)
    parts = lax.all_to_all(pair_sum, LINE_OUTER, 0, 0, tiled=True)
    return parts.sum(axis=0, dtype=value.dtype)


def line_gathered_rows(block):
    outer = lax.axis_size(LINE_OUTER)
    core = lax.axis_index(LINE_CORE)
    copies = jnp.broadcast_to(block[None], (outer, *block.shape))
    mine = lax.all_to_all(copies, LINE_OUTER, 0, 0, tiled=True)
    other = swap_cores(mine)
    whole = jnp.where(core == 0, jnp.stack([mine, other], axis=1), jnp.stack([other, mine], axis=1))
    return whole.reshape(2 * outer * block.shape[0], *block.shape[1:])


def line_full_sum(value):
    return line_gathered_rows(line_summed_block(value))


def dual_update(dual, flow, limit):
    shifted = dual + dual_step * flow
    return shifted - dual_step * jnp.clip(shifted / dual_step, -limit, limit)


def on_device(
    ptdf,
    lodf,
    injection,
    injection_prev,
    bus_cost,
    bus_cap,
    demand,
    balance_dual,
    base_dual,
    post_dual,
    flow_limit,
    emergency_limit,
    outage_line,
    outage_weight,
):
    extrapolated = 2.0 * injection - injection_prev
    extra_high = extrapolated.astype(jnp.bfloat16)
    extra_low = (extrapolated - extra_high.astype(jnp.float32)).astype(jnp.bfloat16)
    stacked = jnp.stack([extra_high, extra_low], axis=0)
    lines_dev = ptdf.shape[0]
    ptdf_turned = ptdf.T
    outer = lax.axis_size(LINE_OUTER)
    line_devs = 2 * outer
    rows = injection.shape[0]
    half = rows - rows // 4

    def flows(portion):
        lead = portion.shape[:-3]
        count = portion.shape[-2]
        flat = portion.reshape(-1, portion.shape[-1])
        product = jnp.dot(flat, ptdf_turned, preferred_element_type=jnp.float32)
        product = product.reshape(*lead, 2, count, lines_dev)
        return product[..., 0, :, :] + product[..., 1, :, :]

    local_total = jnp.sum(extra_high.astype(jnp.float32) + extra_low.astype(jnp.float32), axis=1)
    bus_total = lax.psum(local_total, "col")
    by_gather = lax.all_gather(stacked[:, :half], LINE, axis=1, tiled=True)
    by_gather, bus_total = lax.optimization_barrier((by_gather, bus_total))
    copies = jnp.broadcast_to(stacked[None, :, half:], (outer, *stacked[:, half:].shape))
    mine = lax.all_to_all(copies, LINE_OUTER, 0, 0, tiled=True)
    other = swap_cores(mine)
    core = lax.axis_index(LINE_CORE)
    gather_flow = flows(by_gather).reshape(line_devs, half, lines_dev)
    mine_flow, other_flow = flows(mine), flows(other)
    swap_flow = jnp.where(
        core == 0, jnp.stack([mine_flow, other_flow], axis=1), jnp.stack([other_flow, mine_flow], axis=1)
    ).reshape(line_devs, rows - half, lines_dev)
    flow_part = jnp.concatenate([gather_flow, swap_flow], axis=1).reshape(line_devs * rows, lines_dev)
    base_flow = full_sum(flow_part, "col")
    balance_new = balance_dual + (bus_total - demand) / BUSES
    base_new = dual_update(base_dual, base_flow, flow_limit[None, :])
    first_line = lax.axis_index(LINE) * lines_dev
    local_line = outage_line - first_line
    inside = (local_line >= 0) & (local_line < lines_dev)
    lines_seen = lax.broadcasted_iota(jnp.int32, (lines_dev, outage_line.shape[0]), 0)
    chosen = (lines_seen == local_line[None, :]).astype(jnp.float32)
    exact = lax.Precision.HIGHEST
    outer_devs = lax.axis_size(LINE_OUTER)
    core_now = lax.axis_index(LINE_CORE)
    flow_by_core = base_flow.reshape(outer_devs, 2, base_flow.shape[0] // (2 * outer_devs), lines_dev)

    def weighted(flow_rows):
        picked = jnp.dot(flow_rows, chosen, precision=exact, preferred_element_type=jnp.float32)
        return jnp.where(inside, picked * outage_weight, 0.0).astype(jnp.bfloat16)

    given_out = swap_cores(weighted(jnp.where(core_now == 0, flow_by_core[:, 1], flow_by_core[:, 0])))
    kept_out = lax.optimization_barrier(
        weighted(jnp.where(core_now == 0, flow_by_core[:, 0], flow_by_core[:, 1]))
    )
    outage_parts = lax.all_to_all(kept_out + given_out, LINE_OUTER, 0, 0, tiled=True)
    outage_flow = line_gathered_rows(outage_parts.sum(axis=0, dtype=jnp.bfloat16))
    shift_part = jnp.dot(outage_flow, lodf.T, preferred_element_type=jnp.float32)
    post_shift = full_sum(shift_part, "col")
    post_flow = base_flow + post_shift
    post_new = dual_update(post_dual, post_flow, emergency_limit[None, :])
    back_part = jnp.dot(post_new.astype(jnp.bfloat16), lodf, preferred_element_type=jnp.float32)
    back_flow = line_full_sum(back_part)
    returned_part = lax.dot_general(
        back_flow * outage_weight[None, :],
        chosen,
        (((1,), (1,)), ((), ())),
        precision=exact,
        preferred_element_type=jnp.float32,
    )
    returned = summed_block(returned_part, "col")
    block_rows = returned.shape[0]
    first_row = lax.axis_index("col") * block_rows
    base_block = lax.dynamic_slice_in_dim(base_new, first_row, block_rows, axis=0)
    post_block = lax.dynamic_slice_in_dim(post_new, first_row, block_rows, axis=0)
    line_total = gathered_rows((base_block + post_block + returned).astype(jnp.bfloat16), "col")
    outer_devs = lax.axis_size(LINE_OUTER)
    core_now = lax.axis_index(LINE_CORE)
    by_core = line_total.reshape(outer_devs, 2, line_total.shape[0] // (2 * outer_devs), line_total.shape[1])
    keep_rows = jnp.where(core_now == 0, by_core[:, 0], by_core[:, 1])
    give_rows = jnp.where(core_now == 0, by_core[:, 1], by_core[:, 0])
    given = swap_cores(jnp.dot(give_rows, ptdf, preferred_element_type=jnp.float32))
    kept = lax.optimization_barrier(jnp.dot(keep_rows, ptdf, preferred_element_type=jnp.float32))
    pair_sum = kept + given
    prices = lax.all_to_all(pair_sum, LINE_OUTER, 0, 0, tiled=True).sum(axis=0, dtype=jnp.float32)
    moved = injection - primal_step * (bus_cost[None, :] + prices + balance_new[:, None])
    new_injection = jnp.clip(moved, 0.0, bus_cap[None, :])
    return (new_injection, balance_new, base_new, post_new)


def solution(mesh):
    outer = mesh.shape["line"] // 2
    fine = Mesh(
        mesh.devices.reshape(outer, 2, mesh.shape["col"]), (LINE_OUTER, LINE_CORE, "col")
    )
    in_specs = (
        P(LINE, "col"),
        P(LINE, "col"),
        P(LINE, "col"),
        P(LINE, "col"),
        P("col"),
        P("col"),
        P(LINE),
        P(LINE),
        P(None, LINE),
        P(None, LINE),
        P(LINE),
        P(LINE),
        P("col"),
        P("col"),
    )
    out_specs = (P(LINE, "col"), P(LINE), P(None, LINE), P(None, LINE))

    return jax.shard_map(on_device, mesh=fine, in_specs=in_specs, out_specs=out_specs, check_vma=False)
```
